1024 devices in a mesh: dp: 64 (over z, core), tensor: 16 (over y, x).
Axes of the slice: x: 4, y: 4, z: 32, core: 2. Of those that a mesh axis runs over, the one named last changes fastest.
Arguments:
- inputs: bfloat16 [16384, 2560], P('dp'), may hold values from -16 to 16
- old_weight: bfloat16 [2560, 8192], P('dp', 'tensor'), may hold values from -0.125 to 0.125
- keep_cols: int32 [6144], replicated, may hold values from 0 to 8191, as said below
- owner: int32 [48], replicated, may hold values from 0 to 15, as said below
- out_grad: bfloat16 [16384, 6144], P('dp', 'tensor'), may hold values from -6 to 6
Outputs:
- projected: bfloat16 [16384, 6144], P('dp', 'tensor')
- gradient_input: bfloat16 [16384, 2560], P('dp', 'tensor')
- weight_grad: float32 [2560, 6144], P('dp', 'tensor')
The draws below stay inside these ranges and needn't reach their ends.
Inputs may be any that keep to these rules, and one draw needn't show every extreme that they name: Each index t of tensor holds old columns [t * 4 * 128, (t + 1) * 4 * 128) and keeps exactly 384 of them, so blocks t * 3 to t * 3 + 2 of keep_cols come from holder t. Every owner receives exactly 3 blocks, and at most 2 blocks from one old holder; some owner receives 2 from one holder.
All inputs are finite; a program needn't handle non-finite values.
Results may differ from the reference program's by a relative error of at most 0.015.
Values may be sent and summed in bfloat16 or wider, within the bound.
No kernel may reach another device: no remote copies, remote signals or barrier semaphores. Data moves between devices by JAX's collectives and lax.ppermute only.
A program may use at most 32 MiB of HBM per device.

```python
import jax
import jax.numpy as jnp
from jax import lax

D = 2560
OLD_BLOCKS = 4
NEW_BLOCKS = 3
TOKENS = 16384
FF_OLD = 8192
FF_NEW = 6144
NB = 48
N_TENSOR = 16


def packing_layout(key):
    groups = FF_OLD // (OLD_BLOCKS * 128)
    width_old = OLD_BLOCKS * 128
    blocks = NEW_BLOCKS * groups
    second = jax.random.fold_in(jax.random.fold_in(key, 11), 1)
    third = jax.random.fold_in(jax.random.fold_in(key, 11), 2)
    ranking = jax.vmap(lambda sub: jax.random.permutation(sub, width_old))(jax.random.split(second, groups))
    chosen = ranking < NEW_BLOCKS * 128
    keep = jnp.nonzero(chosen.reshape(-1), size=blocks * 128)[0].astype(jnp.int32)
    sigma = jax.random.permutation(third, groups).astype(jnp.int32)
    index = jnp.arange(blocks, dtype=jnp.int32)
    paired = sigma[jnp.clip(index // 2, 0, groups - 1)]
    single = sigma[jnp.clip(index - 2 * groups, 0, groups - 1)]
    owners = jnp.where(index < 2 * groups, paired, single).astype(jnp.int32)
    return (keep, owners)


def draw_keep_cols(key, part):
    return packing_layout(key)[0]


def draw_owner(key, part):
    return packing_layout(key)[1]


def with_spikes(values, rng, source, target, parts, factor):
    owner, partner = [(jnp.arange(values.shape[position]) // (values.shape[position] // parts)).reshape([-1 if axis == position else 1 for axis in range(values.ndim)]) for position in (source, target)]
    chosen = jax.random.permutation(rng, parts)[partner]
    strong = (owner == chosen) | (owner == (partner + parts // 2) % parts)
    return jnp.where(strong, factor * values, values)


def level_of(own_key, dims, cuts, low, top_value):
    gain = 1.0
    for axis_at, parts in cuts:
        heights = jax.random.uniform(jax.random.fold_in(jax.random.fold_in(own_key, 6), axis_at), (parts,), jnp.float32, low / len(cuts), top_value / len(cuts))
        gain = gain * jnp.repeat(jnp.exp(heights), dims[axis_at] // parts).reshape((-1,) + (1,) * (len(dims) - 1 - axis_at))
    return gain


def centred(stream_key, shape, scale, most, cuts=(), kind=jnp.bfloat16):
    drawn = scale * jax.random.normal(stream_key, shape, jnp.float32)
    if cuts:
        drawn = drawn * level_of(stream_key, shape, cuts, -0.22, 0.18)
    return jnp.clip(drawn, -most, most).astype(kind)


def heavy_noise(rng, shape, deviation, reach, shards, heavy, held_as=jnp.bfloat16):
    array = deviation * jax.random.normal(rng, shape, jnp.float32)
    if shards:
        array = array * level_of(rng, shape, shards, -0.22, 0.18)
    return jnp.clip(with_spikes(array, jax.random.fold_in(rng, 3), *heavy), -reach, reach).astype(held_as)


def setup_inputs(seed: int = 0) -> dict:
    seeds = jax.random.split(jax.random.key(seed), 6)
    return {
        "inputs": heavy_noise(seeds[0], (TOKENS, D), 1.0, 16.0, ((0, 64),), (0, 1, 64, 4.0)),
        "old_weight": centred(seeds[1], (D, FF_OLD), D ** -0.5, 0.125, ((0, 64), (1, 16))),
        "keep_cols": draw_keep_cols(jax.random.fold_in(seeds[5], 71), 0),
        "owner": draw_owner(jax.random.fold_in(seeds[5], 71), 0),
        "out_grad": centred(seeds[4], (TOKENS, FF_NEW), 1.0, 6.0, ((0, 64), (1, 16))),
    }


def reference(inputs, old_weight, keep_cols, owner, out_grad):
    input_rows = inputs.astype(jnp.float32)
    inverse_sigma = lax.rsqrt(lax.optimization_barrier(jnp.mean(input_rows * input_rows, axis=1, keepdims=True)) + 1e-05)
    centered_input = input_rows * inverse_sigma
    normalized_rows = centered_input.astype(jnp.bfloat16)
    order = jnp.argsort(owner, stable=True).astype(jnp.int32)
    columns = keep_cols.reshape(NB, 128)[order].reshape(-1)
    weight = jnp.take(old_weight, columns, axis=1)
    projected = jnp.dot(normalized_rows, weight, preferred_element_type=jnp.float32).astype(jnp.bfloat16)
    share = NEW_BLOCKS * 128
    normalized_gradient = jnp.zeros(input_rows.shape, jnp.float32)
    for group in range(N_TENSOR):
        grad_part = out_grad[:, group * share:(group + 1) * share]
        weight_part = weight[:, group * share:(group + 1) * share]
        partial_term = lax.dot_general(grad_part, weight_part, (((1,), (1,)), ((), ())), preferred_element_type=jnp.float32)
        normalized_gradient = normalized_gradient + partial_term.astype(jnp.bfloat16).astype(jnp.float32)
    inner_product = lax.optimization_barrier(jnp.mean(normalized_gradient * centered_input, axis=1, keepdims=True))
    gradient_input = (inverse_sigma * (normalized_gradient - centered_input * inner_product)).astype(jnp.bfloat16)
    weight_grad = lax.dot_general(normalized_rows, out_grad, (((0,), (0,)), ((), ())), preferred_element_type=jnp.float32)
    return (projected, gradient_input, weight_grad)
```

```python
import jax
import jax.numpy as jnp
from jax import lax
from jax.sharding import Mesh
from jax.sharding import PartitionSpec as P

ZL = 4
DP = ("zh", "zl", "c")
TN = ("y", "x")


def _split_hi_lo(s):
    hi = lax.reduce_precision(s, exponent_bits=8, mantissa_bits=7)
    lo = s - hi
    return hi.astype(jnp.bfloat16), lo.astype(jnp.bfloat16)


def local(inputs, old_weight, keep_cols, owner, out_grad):
    n_t = lax.axis_size(TN)
    n_zh, n_zl, n_c = lax.axis_size("zh"), lax.axis_size("zl"), lax.axis_size("c")
    n_z = n_zh * n_zl
    me = lax.axis_index(TN)
    blocks = owner.shape[0]
    own_blocks = blocks // n_t
    old_cols = old_weight.shape[1]
    rows = old_weight.shape[0]
    tokens, width = inputs.shape
    share = width // n_t

    keep_table = keep_cols.reshape(blocks, 128)
    block_ids = jnp.arange(blocks, dtype=jnp.int32)
    holder_of = block_ids // own_blocks
    earlier = block_ids[None, :] < block_ids[:, None]
    same_pair = (owner[:, None] == owner[None, :]) & (holder_of[:, None] == holder_of[None, :])
    slot_of = jnp.sum(same_pair & earlier, axis=1)
    same_owner = owner[:, None] == owner[None, :]
    owner_rank = jnp.sum(same_owner & earlier, axis=1)

    mine = me * own_blocks + jnp.arange(own_blocks, dtype=jnp.int32)
    dest = jnp.arange(n_t, dtype=jnp.int32)
    slots = jnp.arange(2, dtype=jnp.int32)
    match = (owner[mine][None, None, :] == dest[:, None, None]) & (
        slot_of[mine][None, None, :] == slots[None, :, None]
    )
    pick = jnp.sum(jnp.where(match, mine[None, None, :], 0), axis=2)
    pick = jnp.where(jnp.any(match, axis=2), pick, mine[0])
    local_cols = keep_table[pick] - me * old_cols
    local_cols = jnp.clip(local_cols, 0, old_cols - 1)
    send = jnp.take(old_weight, local_cols.reshape(-1), axis=1).reshape(rows, n_t, 2 * 128)
    send = jnp.transpose(send, (1, 0, 2))
    recv = lax.all_to_all(send, TN, 0, 0, tiled=False)

    k_ids = jnp.arange(own_blocks, dtype=jnp.int32)
    mine_match = (owner[None, :] == me) & (owner_rank[None, :] == k_ids[:, None])
    my_blocks = jnp.sum(jnp.where(mine_match, block_ids[None, :], 0), axis=1)
    h_k = holder_of[my_blocks]
    s_k = slot_of[my_blocks]
    recv4 = recv.reshape(n_t, rows, 2, 128)
    new_stripe = jnp.concatenate(
        [recv4[h_k[k], :, s_k[k], :] for k in range(own_blocks)], axis=1
    )

    piece = lax.all_gather(new_stripe, ("zh", "zl"), axis=0, tiled=True)
    piece = lax.all_gather(piece, "c", axis=0, tiled=True)
    piece = piece.reshape(n_c, n_z, rows, -1).transpose(1, 0, 2, 3).reshape(width, -1)

    x = inputs.astype(jnp.float32)
    inv = lax.rsqrt(jnp.mean(x * x, axis=1, keepdims=True) + 1e-05)
    xhat = x * inv
    normed = xhat.astype(jnp.bfloat16)

    wg = lax.dot_general(normed, out_grad, (((0,), (0,)), ((), ())), preferred_element_type=jnp.float32)
    wg = wg.reshape(n_zh, n_zl, n_c, rows, -1)
    wg = lax.all_to_all(wg, "c", 2, 2, tiled=False).sum(2)
    wg = lax.all_to_all(wg.astype(jnp.bfloat16), "zl", 1, 1, tiled=False).astype(jnp.float32).sum(1)
    wg = lax.all_to_all(wg.astype(jnp.bfloat16), "zh", 0, 0, tiled=False).astype(jnp.float32).sum(0)

    projected = jnp.dot(normed, piece, preferred_element_type=jnp.float32).astype(jnp.bfloat16)

    partial = lax.dot_general(
        out_grad, piece, (((1,), (1,)), ((), ())), preferred_element_type=jnp.float32
    ).astype(jnp.bfloat16)
    s_part = jnp.sum(partial.astype(jnp.float32) * xhat, axis=1)
    hi, lo = _split_hi_lo(s_part)
    extra_len = 4 * share
    extra = jnp.concatenate([hi, lo, jnp.zeros((extra_len - 2 * tokens,), jnp.bfloat16)])
    extra = jnp.broadcast_to(extra.reshape(1, 4, share), (n_t, 4, share))
    payload = jnp.transpose(partial.reshape(tokens, n_t, share), (1, 0, 2))
    payload = jnp.concatenate([payload, extra], axis=1)
    got = lax.all_to_all(payload, TN, 0, 0, tiled=False)
    dn = jnp.sum(got[:, :tokens].astype(jnp.float32), axis=0)
    ex = got[:, tokens:].reshape(n_t, extra_len)
    s_tot = jnp.sum(
        ex[:, :tokens].astype(jnp.float32) + ex[:, tokens:2 * tokens].astype(jnp.float32), axis=0
    )
    inner = (s_tot / width)[:, None]
    xhat_me = lax.dynamic_slice_in_dim(xhat, me * share, share, 1)
    gradient_input = (inv * (dn - xhat_me * inner)).astype(jnp.bfloat16)
    return (projected, gradient_input, wg)


def solution(mesh):
    n_dp, n_t = mesh.devices.shape
    devs = mesh.devices.reshape(n_dp // (2 * ZL), ZL, 2, 4, n_t // 4)
    m = Mesh(devs, ("zh", "zl", "c", "y", "x"))
    placed = (P(DP, None), P(DP, TN), P(), P(), P(DP, TN))
    return jax.shard_map(
        local,
        mesh=m,
        in_specs=placed,
        out_specs=(P(DP, TN), P(DP, TN), P(DP, TN)),
        check_vma=False,
    )
```

```python
import jax
import jax.numpy as jnp
from jax import lax
from jax.sharding import Mesh
from jax.sharding import PartitionSpec as P


ZL = 4
DP = ("zh", "zl", "c")
TN = ("y", "x")


def _split_hi_lo(s):
    hi = lax.reduce_precision(s, exponent_bits=8, mantissa_bits=7)
    lo = s - hi
    return hi.astype(jnp.bfloat16), lo.astype(jnp.bfloat16)


def _body(inputs, old_weight, keep_cols, owner, out_grad):
    n_t = lax.axis_size(TN)
    n_zh, n_zl, n_c = lax.axis_size("zh"), lax.axis_size("zl"), lax.axis_size("c")
    n_z = n_zh * n_zl
    me = lax.axis_index(TN)
    blocks = owner.shape[0]
    own_blocks = blocks // n_t
    old_cols = old_weight.shape[1]
    rows = old_weight.shape[0]
    tokens, width = inputs.shape
    share = width // n_t

    keep_table = keep_cols.reshape(blocks, 128)
    block_ids = jnp.arange(blocks, dtype=jnp.int32)
    holder_of = block_ids // own_blocks
    earlier = block_ids[None, :] < block_ids[:, None]
    same_pair = (owner[:, None] == owner[None, :]) & (holder_of[:, None] == holder_of[None, :])
    slot_of = jnp.sum(same_pair & earlier, axis=1)
    same_owner = owner[:, None] == owner[None, :]
    owner_rank = jnp.sum(same_owner & earlier, axis=1)

    mine = me * own_blocks + jnp.arange(own_blocks, dtype=jnp.int32)
    dest = jnp.arange(n_t, dtype=jnp.int32)
    slots = jnp.arange(2, dtype=jnp.int32)
    match = (owner[mine][None, None, :] == dest[:, None, None]) & (
        slot_of[mine][None, None, :] == slots[None, :, None]
    )
    pick = jnp.sum(jnp.where(match, mine[None, None, :], 0), axis=2)
    pick = jnp.where(jnp.any(match, axis=2), pick, mine[0])
    local_cols = keep_table[pick] - me * old_cols
    local_cols = jnp.clip(local_cols, 0, old_cols - 1)
    onehot = (
        jnp.arange(old_cols, dtype=jnp.int32)[:, None, None] == local_cols.reshape(1, n_t, 256)
    ).astype(old_weight.dtype)
    send = jnp.einsum(
        "rc,ctj->trj", old_weight, onehot, preferred_element_type=jnp.float32
    ).astype(old_weight.dtype)
    recv = lax.all_to_all(send, TN, 0, 0, tiled=False)

    k_ids = jnp.arange(own_blocks, dtype=jnp.int32)
    mine_match = (owner[None, :] == me) & (owner_rank[None, :] == k_ids[:, None])
    my_blocks = jnp.sum(jnp.where(mine_match, block_ids[None, :], 0), axis=1)
    h_k = holder_of[my_blocks]
    s_k = slot_of[my_blocks]
    recv4 = recv.reshape(n_t, rows, 2, 128)
    new_stripe = jnp.concatenate(
        [recv4[h_k[k], :, s_k[k], :] for k in range(own_blocks)], axis=1
    )

    piece = lax.all_gather(new_stripe, ("zh", "zl"), axis=0, tiled=True)
    piece = lax.all_gather(piece, "c", axis=0, tiled=True)
    piece = piece.reshape(n_c, n_z, rows, -1).transpose(1, 0, 2, 3).reshape(width, -1)

    x = inputs.astype(jnp.float32)
    inv = lax.rsqrt(jnp.mean(x * x, axis=1, keepdims=True) + 1e-05)
    xhat = x * inv
    normed = xhat.astype(jnp.bfloat16)

    wg = lax.dot_general(normed, out_grad, (((0,), (0,)), ((), ())), preferred_element_type=jnp.float32)
    wg = wg.reshape(n_zh, n_zl, n_c, rows, -1)
    wg = lax.all_to_all(wg, "c", 2, 2, tiled=False).sum(2)
    wg = lax.all_to_all(wg.astype(jnp.bfloat16), "zl", 1, 1, tiled=False).astype(jnp.float32).sum(1)
    wg = lax.all_to_all(wg.astype(jnp.bfloat16), "zh", 0, 0, tiled=False)
    wg = wg.astype(jnp.float32).sum(0)

    projected = jnp.dot(normed, piece, preferred_element_type=jnp.float32).astype(jnp.bfloat16)

    partial = lax.dot_general(
        out_grad, piece, (((1,), (1,)), ((), ())), preferred_element_type=jnp.float32
    ).astype(jnp.bfloat16)
    s_part = jnp.sum(partial.astype(jnp.float32) * xhat, axis=1)
    hi, lo = _split_hi_lo(s_part)
    extra_len = 4 * share
    extra = jnp.concatenate([hi, lo, jnp.zeros((extra_len - 2 * tokens,), jnp.bfloat16)])
    extra = jnp.broadcast_to(extra.reshape(1, 4, share), (n_t, 4, share))
    payload = jnp.transpose(partial.reshape(tokens, n_t, share), (1, 0, 2))
    payload = jnp.concatenate([payload, extra], axis=1)
    got = lax.all_to_all(payload, TN, 0, 0, tiled=False)
    dn = jnp.sum(got[:, :tokens].astype(jnp.float32), axis=0)
    ex = got[:, tokens:].reshape(n_t, extra_len)
    s_tot = jnp.sum(
        ex[:, :tokens].astype(jnp.float32) + ex[:, tokens:2 * tokens].astype(jnp.float32), axis=0
    )
    inner = (s_tot / width)[:, None]
    xhat_me = lax.dynamic_slice_in_dim(xhat, me * share, share, 1)
    gradient_input = (inv * (dn - xhat_me * inner)).astype(jnp.bfloat16)
    return (projected, gradient_input, wg)


def solution(mesh):
    n_dp, n_t = mesh.devices.shape
    devs = mesh.devices.reshape(n_dp // (2 * ZL), ZL, 2, 4, n_t // 4)
    m = Mesh(devs, ("zh", "zl", "c", "y", "x"))
    placed = (P(DP, None), P(DP, TN), P(), P(), P(DP, TN))
    return jax.shard_map(
        _body,
        mesh=m,
        in_specs=placed,
        out_specs=(P(DP, TN), P(DP, TN), P(DP, TN)),
        check_vma=False,
    )
```

```python
import jax
import jax.numpy as jnp
from jax import lax
from jax.sharding import Mesh
from jax.sharding import PartitionSpec as P


ZL = 4
DP = ("zh", "zl", "c")
TN = ("y", "x")


def _split_hi_lo(s):
    hi = lax.reduce_precision(s, exponent_bits=8, mantissa_bits=7)
    lo = s - hi
    return hi.astype(jnp.bfloat16), lo.astype(jnp.bfloat16)


def _body(inputs, old_weight, keep_cols, owner, out_grad):
    n_t = lax.axis_size(TN)
    n_zh, n_zl, n_c = lax.axis_size("zh"), lax.axis_size("zl"), lax.axis_size("c")
    me = lax.axis_index(TN)
    blocks = owner.shape[0]
    own_blocks = blocks // n_t
    old_cols = old_weight.shape[1]
    rows = old_weight.shape[0]
    tokens, width = inputs.shape
    share = width // n_t

    keep_table = keep_cols.reshape(blocks, 128)
    block_ids = jnp.arange(blocks, dtype=jnp.int32)
    holder_of = block_ids // own_blocks
    earlier = block_ids[None, :] < block_ids[:, None]
    same_pair = (owner[:, None] == owner[None, :]) & (holder_of[:, None] == holder_of[None, :])
    slot_of = jnp.sum(same_pair & earlier, axis=1)
    same_owner = owner[:, None] == owner[None, :]
    owner_rank = jnp.sum(same_owner & earlier, axis=1)

    mine = me * own_blocks + jnp.arange(own_blocks, dtype=jnp.int32)
    dest = jnp.arange(n_t, dtype=jnp.int32)
    slots = jnp.arange(2, dtype=jnp.int32)
    match = (owner[mine][None, None, :] == dest[:, None, None]) & (
        slot_of[mine][None, None, :] == slots[None, :, None]
    )
    pick = jnp.sum(jnp.where(match, mine[None, None, :], 0), axis=2)
    pick = jnp.where(jnp.any(match, axis=2), pick, mine[0])
    local_cols = keep_table[pick] - me * old_cols
    local_cols = jnp.clip(local_cols, 0, old_cols - 1)
    onehot = (
        jnp.arange(old_cols, dtype=jnp.int32)[:, None, None] == local_cols.reshape(1, n_t, 256)
    ).astype(old_weight.dtype)
    send = jnp.einsum(
        "rc,ctj->trj", old_weight, onehot, preferred_element_type=jnp.float32
    ).astype(old_weight.dtype)
    send = jnp.broadcast_to(send[None], (n_c,) + send.shape).reshape(n_c * n_t, rows, 256)
    recv = lax.all_to_all(send, ("c",) + TN, 0, 0, tiled=False)

    k_ids = jnp.arange(own_blocks, dtype=jnp.int32)
    mine_match = (owner[None, :] == me) & (owner_rank[None, :] == k_ids[:, None])
    my_blocks = jnp.sum(jnp.where(mine_match, block_ids[None, :], 0), axis=1)
    h_k = holder_of[my_blocks]
    s_k = slot_of[my_blocks]
    recv5 = recv.reshape(n_c, n_t, rows, 2, 128)
    chip_stripe = jnp.concatenate(
        [recv5[:, h_k[k], :, s_k[k], :] for k in range(own_blocks)], axis=2
    ).reshape(n_c * rows, -1)

    piece = lax.all_gather(chip_stripe, ("zh", "zl"), axis=0, tiled=True)

    x = inputs.astype(jnp.float32)
    inv = lax.rsqrt(jnp.mean(x * x, axis=1, keepdims=True) + 1e-05)
    xhat = x * inv
    normed = xhat.astype(jnp.bfloat16)

    wg = lax.dot_general(normed, out_grad, (((0,), (0,)), ((), ())), preferred_element_type=jnp.float32)
    wg, _ = lax.optimization_barrier((wg, chip_stripe))
    wg = wg.reshape(n_zh, n_zl, n_c, rows, -1)
    wg = lax.all_to_all(wg, "c", 2, 2, tiled=False).sum(2)
    wg = lax.all_to_all(wg.astype(jnp.bfloat16), "zl", 1, 1, tiled=False).astype(jnp.float32).sum(1)
    wg = lax.all_to_all(wg.astype(jnp.bfloat16), "zh", 0, 0, tiled=False)
    wg = wg.astype(jnp.float32).sum(0)

    projected = jnp.dot(normed, piece, preferred_element_type=jnp.float32).astype(jnp.bfloat16)

    partial = lax.dot_general(
        out_grad, piece, (((1,), (1,)), ((), ())), preferred_element_type=jnp.float32
    ).astype(jnp.bfloat16)
    s_part = jnp.sum(partial.astype(jnp.float32) * xhat, axis=1)
    hi, lo = _split_hi_lo(s_part)
    extra_len = 4 * share
    extra = jnp.concatenate([hi, lo, jnp.zeros((extra_len - 2 * tokens,), jnp.bfloat16)])
    extra = jnp.broadcast_to(extra.reshape(1, 4, share), (n_t, 4, share))
    payload = jnp.transpose(partial.reshape(tokens, n_t, share), (1, 0, 2))
    payload = jnp.concatenate([payload, extra], axis=1)
    got = lax.all_to_all(payload, TN, 0, 0, tiled=False)
    dn = jnp.sum(got[:, :tokens].astype(jnp.float32), axis=0)
    ex = got[:, tokens:].reshape(n_t, extra_len)
    s_tot = jnp.sum(
        ex[:, :tokens].astype(jnp.float32) + ex[:, tokens:2 * tokens].astype(jnp.float32), axis=0
    )
    inner = (s_tot / width)[:, None]
    xhat_me = lax.dynamic_slice_in_dim(xhat, me * share, share, 1)
    gradient_input = (inv * (dn - xhat_me * inner)).astype(jnp.bfloat16)
    return (projected, gradient_input, wg)


def solution(mesh):
    n_dp, n_t = mesh.devices.shape
    devs = mesh.devices.reshape(n_dp // (2 * ZL), ZL, 2, 4, n_t // 4)
    m = Mesh(devs, ("zh", "zl", "c", "y", "x"))
    placed = (P(DP, None), P(DP, TN), P(), P(), P(DP, TN))
    return jax.shard_map(
        _body,
        mesh=m,
        in_specs=placed,
        out_specs=(P(DP, TN), P(DP, TN), P(DP, TN)),
        check_vma=False,
    )
```

```python
import jax
import jax.numpy as jnp
from jax import lax
from jax.sharding import Mesh
from jax.sharding import PartitionSpec as P


ZL = 4
DP = ("zh", "zl", "c")
TN = ("y", "x")


def _split_hi_lo(s):
    hi = lax.reduce_precision(s, exponent_bits=8, mantissa_bits=7)
    lo = s - hi
    return hi.astype(jnp.bfloat16), lo.astype(jnp.bfloat16)


def _body(inputs, old_weight, keep_cols, owner, out_grad):
    n_t = lax.axis_size(TN)
    n_zh, n_zl, n_c = lax.axis_size("zh"), lax.axis_size("zl"), lax.axis_size("c")
    n_z = n_zh * n_zl
    me = lax.axis_index(TN)
    blocks = owner.shape[0]
    own_blocks = blocks // n_t
    old_cols = old_weight.shape[1]
    rows = old_weight.shape[0]
    tokens, width = inputs.shape
    share = width // n_t

    keep_table = keep_cols.reshape(blocks, 128)
    block_ids = jnp.arange(blocks, dtype=jnp.int32)
    holder_of = block_ids // own_blocks
    earlier = block_ids[None, :] < block_ids[:, None]
    same_pair = (owner[:, None] == owner[None, :]) & (holder_of[:, None] == holder_of[None, :])
    slot_of = jnp.sum(same_pair & earlier, axis=1)
    same_owner = owner[:, None] == owner[None, :]
    owner_rank = jnp.sum(same_owner & earlier, axis=1)

    mine = me * own_blocks + jnp.arange(own_blocks, dtype=jnp.int32)
    dest = jnp.arange(n_t, dtype=jnp.int32)
    slots = jnp.arange(2, dtype=jnp.int32)
    match = (owner[mine][None, None, :] == dest[:, None, None]) & (
        slot_of[mine][None, None, :] == slots[None, :, None]
    )
    pick = jnp.sum(jnp.where(match, mine[None, None, :], 0), axis=2)
    pick = jnp.where(jnp.any(match, axis=2), pick, mine[0])
    local_cols = keep_table[pick] - me * old_cols
    local_cols = jnp.clip(local_cols, 0, old_cols - 1)
    onehot = (
        jnp.arange(old_cols, dtype=jnp.int32)[:, None, None] == local_cols.reshape(1, n_t, 256)
    ).astype(old_weight.dtype)
    send = jnp.einsum(
        "rc,ctj->trj", old_weight, onehot, preferred_element_type=jnp.float32
    ).astype(old_weight.dtype)
    recv = lax.all_to_all(send, TN, 0, 0, tiled=False)

    k_ids = jnp.arange(own_blocks, dtype=jnp.int32)
    mine_match = (owner[None, :] == me) & (owner_rank[None, :] == k_ids[:, None])
    my_blocks = jnp.sum(jnp.where(mine_match, block_ids[None, :], 0), axis=1)
    h_k = holder_of[my_blocks]
    s_k = slot_of[my_blocks]
    recv4 = recv.reshape(n_t, rows, 2, 128)
    new_stripe = jnp.concatenate(
        [recv4[h_k[k], :, s_k[k], :] for k in range(own_blocks)], axis=1
    )

    piece = lax.all_gather(new_stripe, ("zh", "zl"), axis=0, tiled=True)
    piece = jnp.broadcast_to(piece[None], (n_c,) + piece.shape)
    piece = lax.all_to_all(piece, "c", 0, 0, tiled=False)
    piece = piece.reshape(n_c, n_z, rows, -1).transpose(1, 0, 2, 3).reshape(width, -1)

    x = inputs.astype(jnp.float32)
    inv = lax.rsqrt(jnp.mean(x * x, axis=1, keepdims=True) + 1e-05)
    xhat = x * inv
    normed = xhat.astype(jnp.bfloat16)

    wg = lax.dot_general(normed, out_grad, (((0,), (0,)), ((), ())), preferred_element_type=jnp.float32)
    wg = wg.reshape(n_zh, n_zl, n_c, rows, -1)
    wg = lax.all_to_all(wg.astype(jnp.bfloat16), "c", 2, 2, tiled=False).astype(jnp.float32).sum(2)
    wg = lax.all_to_all(wg.astype(jnp.bfloat16), "zl", 1, 1, tiled=False).astype(jnp.float32).sum(1)
    wg = lax.all_to_all(wg.astype(jnp.bfloat16), "zh", 0, 0, tiled=False)
    wg = wg.astype(jnp.float32).sum(0)

    projected = jnp.dot(normed, piece, preferred_element_type=jnp.float32).astype(jnp.bfloat16)

    partial = lax.dot_general(
        out_grad, piece, (((1,), (1,)), ((), ())), preferred_element_type=jnp.float32
    ).astype(jnp.bfloat16)
    s_part = jnp.sum(partial.astype(jnp.float32) * xhat, axis=1)
    hi, lo = _split_hi_lo(s_part)
    extra_len = 4 * share
    extra = jnp.concatenate([hi, lo, jnp.zeros((extra_len - 2 * tokens,), jnp.bfloat16)])
    extra = jnp.broadcast_to(extra.reshape(1, 4, share), (n_t, 4, share))
    payload = jnp.transpose(partial.reshape(tokens, n_t, share), (1, 0, 2))
    payload = jnp.concatenate([payload, extra], axis=1)
    got = lax.all_to_all(payload, TN, 0, 0, tiled=False)
    dn = jnp.sum(got[:, :tokens].astype(jnp.float32), axis=0)
    ex = got[:, tokens:].reshape(n_t, extra_len)
    s_tot = jnp.sum(
        ex[:, :tokens].astype(jnp.float32) + ex[:, tokens:2 * tokens].astype(jnp.float32), axis=0
    )
    inner = (s_tot / width)[:, None]
    xhat_me = lax.dynamic_slice_in_dim(xhat, me * share, share, 1)
    gradient_input = (inv * (dn - xhat_me * inner)).astype(jnp.bfloat16)
    return (projected, gradient_input, wg)


def solution(mesh):
    n_dp, n_t = mesh.devices.shape
    devs = mesh.devices.reshape(n_dp // (2 * ZL), ZL, 2, 4, n_t // 4)
    m = Mesh(devs, ("zh", "zl", "c", "y", "x"))
    placed = (P(DP, None), P(DP, TN), P(), P(), P(DP, TN))
    return jax.shard_map(
        _body,
        mesh=m,
        in_specs=placed,
        out_specs=(P(DP, TN), P(DP, TN), P(DP, TN)),
        check_vma=False,
    )
```

```python
import jax
import jax.numpy as jnp
from jax import lax
from jax.sharding import Mesh
from jax.sharding import PartitionSpec as P


ZL = 4
DP = ("zh", "zl", "c")
TN = ("y", "x")


def _split_hi_lo(s):
    hi = lax.reduce_precision(s, exponent_bits=8, mantissa_bits=7)
    lo = s - hi
    return hi.astype(jnp.bfloat16), lo.astype(jnp.bfloat16)


def _body(inputs, old_weight, keep_cols, owner, out_grad):
    n_t = lax.axis_size(TN)
    n_zh, n_zl, n_c = lax.axis_size("zh"), lax.axis_size("zl"), lax.axis_size("c")
    n_z = n_zh * n_zl
    me = lax.axis_index(TN)
    blocks = owner.shape[0]
    own_blocks = blocks // n_t
    old_cols = old_weight.shape[1]
    rows = old_weight.shape[0]
    tokens, width = inputs.shape
    share = width // n_t

    keep_table = keep_cols.reshape(blocks, 128)
    block_ids = jnp.arange(blocks, dtype=jnp.int32)
    holder_of = block_ids // own_blocks
    earlier = block_ids[None, :] < block_ids[:, None]
    same_pair = (owner[:, None] == owner[None, :]) & (holder_of[:, None] == holder_of[None, :])
    slot_of = jnp.sum(same_pair & earlier, axis=1)
    same_owner = owner[:, None] == owner[None, :]
    owner_rank = jnp.sum(same_owner & earlier, axis=1)

    mine = me * own_blocks + jnp.arange(own_blocks, dtype=jnp.int32)
    dest = jnp.arange(n_t, dtype=jnp.int32)
    slots = jnp.arange(2, dtype=jnp.int32)
    match = (owner[mine][None, None, :] == dest[:, None, None]) & (
        slot_of[mine][None, None, :] == slots[None, :, None]
    )
    pick = jnp.sum(jnp.where(match, mine[None, None, :], 0), axis=2)
    pick = jnp.where(jnp.any(match, axis=2), pick, mine[0])
    local_cols = keep_table[pick] - me * old_cols
    local_cols = jnp.clip(local_cols, 0, old_cols - 1)
    onehot = (
        jnp.arange(old_cols, dtype=jnp.int32)[:, None, None] == local_cols.reshape(1, n_t, 256)
    ).astype(old_weight.dtype)
    send = jnp.einsum(
        "rc,ctj->trj", old_weight, onehot, preferred_element_type=jnp.float32
    ).astype(old_weight.dtype)
    recv = lax.all_to_all(send, TN, 0, 0, tiled=False)

    k_ids = jnp.arange(own_blocks, dtype=jnp.int32)
    mine_match = (owner[None, :] == me) & (owner_rank[None, :] == k_ids[:, None])
    my_blocks = jnp.sum(jnp.where(mine_match, block_ids[None, :], 0), axis=1)
    h_k = holder_of[my_blocks]
    s_k = slot_of[my_blocks]
    recv4 = recv.reshape(n_t, rows, 2, 128)
    new_stripe = jnp.concatenate(
        [recv4[h_k[k], :, s_k[k], :] for k in range(own_blocks)], axis=1
    )

    piece = lax.all_gather(new_stripe, ("zh", "zl"), axis=0, tiled=True)
    piece = jnp.broadcast_to(piece[None], (n_c,) + piece.shape)
    piece = lax.all_to_all(piece, "c", 0, 0, tiled=False)
    piece = piece.reshape(n_c, n_z, rows, -1).transpose(1, 0, 2, 3).reshape(width, -1)

    x = inputs.astype(jnp.float32)
    inv = lax.rsqrt(jnp.mean(x * x, axis=1, keepdims=True) + 1e-05)
    xhat = x * inv
    normed = xhat.astype(jnp.bfloat16)

    wg = lax.dot_general(normed, out_grad, (((0,), (0,)), ((), ())), preferred_element_type=jnp.float32)
    wg = wg.reshape(n_zh, n_zl * n_c, rows, -1)
    wg = lax.all_to_all(wg.astype(jnp.bfloat16), ("zl", "c"), 1, 1, tiled=False).astype(jnp.float32).sum(1)
    wg = lax.all_to_all(wg.astype(jnp.bfloat16), "zh", 0, 0, tiled=False)
    wg = wg.astype(jnp.float32).sum(0)

    projected = jnp.dot(normed, piece, preferred_element_type=jnp.float32).astype(jnp.bfloat16)

    partial = lax.dot_general(
        out_grad, piece, (((1,), (1,)), ((), ())), preferred_element_type=jnp.float32
    ).astype(jnp.bfloat16)
    s_part = jnp.sum(partial.astype(jnp.float32) * xhat, axis=1)
    hi, lo = _split_hi_lo(s_part)
    extra_len = 4 * share
    extra = jnp.concatenate([hi, lo, jnp.zeros((extra_len - 2 * tokens,), jnp.bfloat16)])
    extra = jnp.broadcast_to(extra.reshape(1, 4, share), (n_t, 4, share))
    payload = jnp.transpose(partial.reshape(tokens, n_t, share), (1, 0, 2))
    payload = jnp.concatenate([payload, extra], axis=1)
    got = lax.all_to_all(payload, TN, 0, 0, tiled=False)
    dn = jnp.sum(got[:, :tokens].astype(jnp.float32), axis=0)
    ex = got[:, tokens:].reshape(n_t, extra_len)
    s_tot = jnp.sum(
        ex[:, :tokens].astype(jnp.float32) + ex[:, tokens:2 * tokens].astype(jnp.float32), axis=0
    )
    inner = (s_tot / width)[:, None]
    xhat_me = lax.dynamic_slice_in_dim(xhat, me * share, share, 1)
    gradient_input = (inv * (dn - xhat_me * inner)).astype(jnp.bfloat16)
    return (projected, gradient_input, wg)


def solution(mesh):
    n_dp, n_t = mesh.devices.shape
    devs = mesh.devices.reshape(n_dp // (2 * ZL), ZL, 2, 4, n_t // 4)
    m = Mesh(devs, ("zh", "zl", "c", "y", "x"))
    placed = (P(DP, None), P(DP, TN), P(), P(), P(DP, TN))
    return jax.shard_map(
        _body,
        mesh=m,
        in_specs=placed,
        out_specs=(P(DP, TN), P(DP, TN), P(DP, TN)),
        check_vma=False,
    )
```
